32 devices in a mesh: series: 4 (over y, x), tm: 8 (over z, core).
Axes of the slice: x: 2, y: 2, z: 4, core: 2. Of those that a mesh axis runs over, the one named last changes fastest.
Arguments:
- panel: bfloat16 [8192, 2048], P('series', 'tm'), may hold values from -6 to 6
- observed: int32 [8192, 256], P('series', 'tm'), may hold values from 0 to 255
- series_factors: float32 [8192, 128], P(('series', 'tm')), may hold values from -2 to 2
- time_factors: float32 [128, 2048], P(None, 'tm'), may hold values from -6 to 6
- ar_weights: float32 [25, 128], replicated, may hold values from -0.06 to 0.06
- lags: int32 [25], replicated, may hold values from 1 to 168, as said below
Outputs:
- factors_next: float32 [8192, 128], P(('series', 'tm'))
- times_next: float32 [128, 2048], P(None, 'tm')
- misfit_final: bfloat16 [8192, 2048], P('series', 'tm')
The draws below stay inside these ranges and needn't reach their ends.
Inputs may be any that keep to these rules, and one draw needn't show every extreme that they name: lags rise strictly; the first is 1 and the last is 168.
All inputs are finite; a program needn't handle non-finite values.
Results may differ from the reference program's by a relative error of at most 0.0047.
Values may be sent and summed in bfloat16 or wider, within the bound.
No kernel may reach another device: no remote copies, remote signals or barrier semaphores. Data moves between devices by JAX's collectives and lax.ppermute only.
A program may use at most 64 MiB of HBM per device.

```python
import jax
import jax.numpy as jnp
from jax import lax

RANK = 128
NLAG = 25
MAXLAG = 168
ITERS = 2
SER_DEV = 2048
TOTAL_SERIES = 8192
TOTAL_HOURS = 2048
WORDS = 256
N_SERIES = 4


def draw_lags(key, part):
    middle = jax.random.permutation(key, MAXLAG - 2)[:NLAG - 2] + 2
    middle = jnp.sort(middle.astype(jnp.int32))
    first = jnp.array([1], dtype=jnp.int32)
    last = jnp.array([MAXLAG], dtype=jnp.int32)
    return jnp.concatenate([first, middle, last]).astype(jnp.int32)


def place_ends(drawn, key, smallest, high):
    shape = drawn.shape
    place = [jax.random.randint(jax.random.fold_in(key, axis), (), 0, shape[axis]) for axis in range(len(shape))]
    drawn = drawn.at[tuple(place)].set(smallest)
    longest = shape.index(max(shape))
    place[longest] = (place[longest] + 1) % shape[longest]
    return drawn.at[tuple(place)].set(high)


def with_spikes(values, own_key, source, target, blocks, factor):
    def block_of(axis_at):
        return (jnp.arange(values.shape[axis_at]) // (values.shape[axis_at] // blocks)).reshape((-1,) + (1,) * (values.ndim - 1 - axis_at))

    near = jax.random.permutation(own_key, blocks)[block_of(target)]
    far = (block_of(target) + blocks // 2) % blocks
    return jnp.where((block_of(source) == near) | (block_of(source) == far), factor * values, values)


def shard_levels(own_key, dims, cuts, low, largest):
    loudness, own = 1.0, jax.random.fold_in(own_key, 6)
    for axis_at, shards_of in cuts:
        draws = jnp.exp(jax.random.uniform(jax.random.fold_in(own, axis_at), (shards_of,), jnp.float32, low / len(cuts), largest / len(cuts)))
        loudness = loudness * jnp.repeat(draws, dims[axis_at] // shards_of).reshape([-1 if axis == axis_at else 1 for axis in range(len(dims))])
    return loudness


def centred(own_key, dims, spread, limit, cuts=(), kind=jnp.bfloat16):
    level = shard_levels(own_key, dims, cuts, -0.22, 0.18) if cuts else 1.0
    values = jax.random.normal(own_key, dims, jnp.float32) * spread * level
    return jnp.minimum(jnp.maximum(values, -limit), limit).astype(kind)


def noise_with(stream_key, shape, deviation, most, split, heavy, held_as=jnp.bfloat16):
    result = deviation * jax.random.normal(stream_key, shape, jnp.float32)
    if split:
        result = result * shard_levels(stream_key, shape, split, -0.22, 0.18)
    return jnp.clip(with_spikes(result, jax.random.fold_in(stream_key, 3), *heavy), -most, most).astype(held_as)


def setup_inputs(seed: int = 0) -> dict:
    key_of = jax.random.split(jax.random.key(seed), 7)
    panel = noise_with(key_of[0], (TOTAL_SERIES, TOTAL_HOURS), 1.0, 6.0, ((0, 4), (1, 8)), (1, 0, 8, 2.0))
    observed = place_ends(jax.random.randint(key_of[1], (TOTAL_SERIES, WORDS), 0, 256), jax.random.fold_in(key_of[1], 1), 0, 255).astype(jnp.int32)
    series_factors = centred(key_of[2], (TOTAL_SERIES, RANK), 0.15, 2.0, ((0, 32),), jnp.float32)
    time_factors = centred(key_of[3], (RANK, TOTAL_HOURS), 0.5, 6.0, ((1, 8),), jnp.float32)
    ar_weights = jnp.clip(jax.random.uniform(key_of[4], (NLAG, RANK), jnp.float32, -0.06, 0.06), -0.06, 0.06)
    lags = draw_lags(jax.random.fold_in(key_of[6], 71), 0)
    return dict(panel=panel, observed=observed, series_factors=series_factors, time_factors=time_factors, ar_weights=ar_weights, lags=lags)


def unpack(packed_words):
    shift_amounts = jnp.arange(8, dtype=jnp.int32)
    bit_values = jnp.right_shift(packed_words[:, :, None], shift_amounts) & 1
    return bit_values.reshape(packed_words.shape[0], packed_words.shape[1] * 8).astype(jnp.float32)


def lagged_before(extended, weights, lags, width):
    def add_lag(lag_index, running_sum):
        offset_start = (MAXLAG - lags[lag_index]).astype(jnp.int32)
        column_block = lax.dynamic_slice_in_dim(extended, offset_start, width, 1)
        return running_sum + weights[lag_index][:, None] * column_block
    return lax.fori_loop(0, lags.shape[0], add_lag, jnp.zeros((extended.shape[0], width), jnp.float32))


def lagged_after(extended, weights, lags, width):
    def add_lag(lag_index, running_sum):
        offset_start = lags[lag_index].astype(jnp.int32)
        column_block = lax.dynamic_slice_in_dim(extended, offset_start, width, 1)
        return running_sum + weights[lag_index][:, None] * column_block
    return lax.fori_loop(0, lags.shape[0], add_lag, jnp.zeros((extended.shape[0], width), jnp.float32))


def ar_gradient(times, weights, lags):
    padding = jnp.zeros((times.shape[0], MAXLAG), jnp.float32)
    errors = times - lagged_before(jnp.concatenate([padding, times], 1), weights, lags, TOTAL_HOURS)
    hour_index = jnp.arange(TOTAL_HOURS, dtype=jnp.int32)
    errors = jnp.where(hour_index[None, :] >= MAXLAG, errors, 0.0)
    return errors - lagged_after(jnp.concatenate([errors, padding], 1), weights, lags, TOTAL_HOURS)


def misfit_block(rows_low, times_low, panel_block, word_block):
    predicted = jnp.dot(rows_low, times_low, preferred_element_type=jnp.float32)
    return (unpack(word_block) * (predicted - panel_block.astype(jnp.float32))).astype(jnp.bfloat16)


def reference(panel, observed, series_factors, time_factors, ar_weights, lags):
    panel_blocks = panel.reshape(N_SERIES, SER_DEV, TOTAL_HOURS)
    word_blocks = observed.reshape(N_SERIES, SER_DEV, WORDS)
    factors = series_factors
    times = time_factors
    for iteration in range(ITERS):
        rows_low = factors.astype(jnp.bfloat16)
        times_low = times.astype(jnp.bfloat16)

        def block_step(running, inputs_block):
            panel_block, word_block, rows_block = inputs_block
            misfit = misfit_block(rows_block, times_low, panel_block, word_block)
            grad_rows = lax.dot_general(misfit, times_low, (((1,), (1,)), ((), ())), preferred_element_type=jnp.float32)
            running = running + lax.dot_general(rows_block, misfit, (((0,), (0,)), ((), ())), preferred_element_type=jnp.float32)
            return running, grad_rows

        grad_times, grad_rows = lax.scan(block_step, jnp.zeros((RANK, TOTAL_HOURS), jnp.float32),
                                         (panel_blocks, word_blocks, rows_low.reshape(N_SERIES, SER_DEV, RANK)))
        ar_grad = ar_gradient(times, ar_weights, lags)
        factors = factors - (2.0 / TOTAL_HOURS) * grad_rows.reshape(TOTAL_SERIES, RANK)
        times = times - (24.0 / TOTAL_SERIES) * grad_times - 0.25 * ar_grad
    rows_low = factors.astype(jnp.bfloat16).reshape(N_SERIES, SER_DEV, RANK)
    times_low = times.astype(jnp.bfloat16)

    def final_block(inputs_block):
        panel_block, word_block, rows_block = inputs_block
        return misfit_block(rows_block, times_low, panel_block, word_block)

    misfit_final = lax.map(final_block, (panel_blocks, word_blocks, rows_low))
    return factors, times, misfit_final.reshape(TOTAL_SERIES, TOTAL_HOURS)
```

```python
import jax
import jax.numpy as jnp
from jax import lax
from jax.sharding import PartitionSpec as P

MAXLAG = 168
ITERS = 2


def shifted(block, axis, distance):
    devices = range(lax.axis_size(axis))
    route = [(i - distance, i) for i in devices if i - distance in devices]
    return lax.ppermute(block, axis, route)


def unpack(packed_words):
    shift_amounts = jnp.arange(8, dtype=jnp.int32)
    bit_values = jnp.right_shift(packed_words[:, :, None], shift_amounts) & 1
    return bit_values.reshape(packed_words.shape[0], packed_words.shape[1] * 8).astype(jnp.float32)


def lagged_before(extended, weights, lags, width):

    def add_lag(lag_index, running_sum):
        offset_start = MAXLAG - lags[lag_index]
        column_block = lax.dynamic_slice_in_dim(extended, offset_start, width, 1)
        return running_sum + weights[lag_index][:, None] * column_block

    running = jnp.zeros((extended.shape[0], width), jnp.float32)
    for k in range(lags.shape[0]):
        running = add_lag(k, running)
    return running


def lagged_after(extended, weights, lags, width):

    def add_lag(lag_index, running_sum):
        offset_start = lags[lag_index]
        column_block = lax.dynamic_slice_in_dim(extended, offset_start, width, 1)
        return running_sum + weights[lag_index][:, None] * column_block

    running = jnp.zeros((extended.shape[0], width), jnp.float32)
    for k in range(lags.shape[0]):
        running = add_lag(k, running)
    return running


def fetch_rows(factors):
    return lax.all_gather(factors.astype(jnp.bfloat16), "tm", axis=0, tiled=True)


def local(panel, observed, series_factors, time_factors, ar_weights, lags):
    hours = panel.shape[1]
    total_hours = hours * lax.axis_size("tm")
    total_series = panel.shape[0] * lax.axis_size("series")
    mask_values = unpack(observed)
    position = lax.axis_index("tm")
    hour_index = position * hours + jnp.arange(hours, dtype=jnp.int32)
    active_mask = (hour_index >= MAXLAG)[None, :]

    def compute_misfit(rows_low, times_low):
        predicted = jnp.dot(rows_low, times_low, preferred_element_type=jnp.float32)
        return (mask_values * (predicted - panel.astype(jnp.float32))).astype(jnp.bfloat16)

    times = time_factors
    factors = series_factors
    for iteration in range(ITERS):
        rows_low = fetch_rows(factors)
        times_low = times.astype(jnp.bfloat16)
        misfit = compute_misfit(rows_low, times_low)
        grad_rows = lax.psum_scatter(
            lax.dot_general(
                misfit, times_low, (((1,), (1,)), ((), ())), preferred_element_type=jnp.float32
            ),
            "tm",
            scatter_dimension=0,
            tiled=True,
        )
        partial_value = lax.dot_general(
            rows_low, misfit, (((0,), (0,)), ((), ())), preferred_element_type=jnp.float32
        )
        grad_times = lax.psum(partial_value, "series")
        tail_cols = shifted(times[:, hours - MAXLAG :], "tm", 1)
        errors = times - lagged_before(
            jnp.concatenate([tail_cols, times], 1), ar_weights, lags, hours
        )
        errors = jnp.where(active_mask, errors, 0.0)
        head_cols = shifted(errors[:, :MAXLAG], "tm", -1)
        ar_grad = errors - lagged_after(
            jnp.concatenate([errors, head_cols], 1), ar_weights, lags, hours
        )
        times_new = times - 24.0 / total_series * grad_times - 0.25 * ar_grad
        factors = factors - 2.0 / total_hours * grad_rows
        times = times_new
    final_rows = fetch_rows(factors)
    misfit_final = compute_misfit(final_rows, times.astype(jnp.bfloat16))
    return (factors, times, misfit_final)


def solution(mesh):
    in_specs = (
        P("series", "tm"),
        P("series", "tm"),
        P(("series", "tm"), None),
        P(None, "tm"),
        P(),
        P(),
    )
    out_specs = (P(("series", "tm"), None), P(None, "tm"), P("series", "tm"))
    return jax.shard_map(local, mesh=mesh, in_specs=in_specs, out_specs=out_specs, check_vma=False)
```

```python
import jax
import jax.numpy as jnp
from jax import lax
from jax.experimental import pallas as pl
from jax.experimental.pallas import tpu as pltpu
from jax.sharding import PartitionSpec as P

MAXLAG = 168
ITERS = 2


def shifted(block, axis, distance):
    devices = range(lax.axis_size(axis))
    route = [(i - distance, i) for i in devices if i - distance in devices]
    return lax.ppermute(block, axis, route)


def exchange(block, axis, bit):
    devices = lax.axis_size(axis)
    return lax.ppermute(block, axis, [(i, i ^ bit) for i in range(devices)])


def butterfly_sum(block, axis):
    devices = lax.axis_size(axis)
    bit = 1
    while bit < devices:
        block = block + exchange(block, axis, bit)
        bit *= 2
    return block


def halving_sum(block, axis):
    devices = lax.axis_size(axis)
    position = lax.axis_index(axis)
    levels = devices.bit_length() - 1
    rows = block.shape[0] // devices
    block = block.reshape((2,) * levels + (rows,) + block.shape[1:])
    for level in range(levels):
        bit = 1 << level
        upper = (position & bit) != 0
        at = levels - 1 - level
        low = lax.index_in_dim(block, 0, at, keepdims=False)
        high = lax.index_in_dim(block, 1, at, keepdims=False)
        keep = jnp.where(upper, high, low)
        send = jnp.where(upper, low, high)
        block = keep + exchange(send, axis, bit)
    return block


def doubling_gather(block, axis):
    devices = lax.axis_size(axis)
    position = lax.axis_index(axis)
    levels = devices.bit_length() - 1
    for step in range(levels):
        bit = 1 << (levels - 1 - step)
        upper = (position & bit) != 0
        other = exchange(block, axis, bit)
        low = jnp.where(upper, other, block)
        high = jnp.where(upper, block, other)
        block = jnp.stack([low, high], axis=step)
    return block.reshape((-1,) + block.shape[levels + 1 :])


def unpack(packed_words):
    shift_amounts = jnp.arange(8, dtype=jnp.int32)
    bit_values = jnp.right_shift(packed_words[:, :, None], shift_amounts) & 1
    return bit_values.reshape(packed_words.shape[0], packed_words.shape[1] * 8).astype(jnp.float32)


def lag_kernel(starts_ref, weights_ref, extended_ref, out_ref):
    width = out_ref.shape[0]
    running = jnp.zeros(out_ref.shape, jnp.float32)
    for k in range(weights_ref.shape[0]):
        row_block = extended_ref[pl.ds(starts_ref[k], width), :]
        running = running + weights_ref[pl.ds(k, 1), :] * row_block
    out_ref[...] = running


def lagged_sum(extended, weights, starts, width):
    rank = extended.shape[1]
    return pl.pallas_call(
        lag_kernel,
        out_shape=jax.ShapeDtypeStruct((width, rank), jnp.float32),
        in_specs=[
            pl.BlockSpec(memory_space=pltpu.SMEM),
            pl.BlockSpec(memory_space=pltpu.VMEM),
            pl.BlockSpec(memory_space=pltpu.VMEM),
        ],
        out_specs=pl.BlockSpec(memory_space=pltpu.VMEM),
        cost_estimate=pl.CostEstimate(
            flops=2 * weights.shape[0] * width * rank,
            transcendentals=0,
            bytes_accessed=4 * (extended.size + weights.size + width * rank),
        ),
    )(starts.astype(jnp.int32), weights, extended)


def fetch_rows(factors):
    return doubling_gather(factors.astype(jnp.bfloat16), "tm")


def local(panel, observed, series_factors, time_factors, ar_weights, lags):
    hours = panel.shape[1]
    total_hours = hours * lax.axis_size("tm")
    total_series = panel.shape[0] * lax.axis_size("series")
    mask_values = unpack(observed)
    position = lax.axis_index("tm")
    hour_index = position * hours + jnp.arange(hours, dtype=jnp.int32)
    active_rows = (hour_index >= MAXLAG)[:, None]

    def compute_misfit(rows_low, times_low):
        predicted = jnp.dot(rows_low, times_low, preferred_element_type=jnp.float32)
        return (mask_values * (predicted - panel.astype(jnp.float32))).astype(jnp.bfloat16)

    times = time_factors
    factors = series_factors
    for iteration in range(ITERS):
        rows_low = fetch_rows(factors)
        times_low = times.astype(jnp.bfloat16)
        misfit = compute_misfit(rows_low, times_low)
        grad_rows = halving_sum(
            lax.dot_general(
                misfit, times_low, (((1,), (1,)), ((), ())), preferred_element_type=jnp.float32
            ),
            "tm",
        )
        partial_value = lax.dot_general(
            rows_low, misfit, (((0,), (0,)), ((), ())), preferred_element_type=jnp.float32
        )
        grad_times = butterfly_sum(partial_value, "series")
        times_t = times.T
        tail_rows = shifted(times_t[hours - MAXLAG :], "tm", 1)
        errors = times_t - lagged_sum(
            jnp.concatenate([tail_rows, times_t], 0), ar_weights, MAXLAG - lags, hours
        )
        errors = jnp.where(active_rows, errors, 0.0)
        head_rows = shifted(errors[:MAXLAG], "tm", -1)
        ar_grad = (errors - lagged_sum(
            jnp.concatenate([errors, head_rows], 0), ar_weights, lags, hours
        )).T
        times_new = times - 24.0 / total_series * grad_times - 0.25 * ar_grad
        factors = factors - 2.0 / total_hours * grad_rows
        times = times_new
    final_rows = fetch_rows(factors)
    misfit_final = compute_misfit(final_rows, times.astype(jnp.bfloat16))
    return (factors, times, misfit_final)


def solution(mesh):
    in_specs = (
        P("series", "tm"),
        P("series", "tm"),
        P(("series", "tm"), None),
        P(None, "tm"),
        P(),
        P(),
    )
    out_specs = (P(("series", "tm"), None), P(None, "tm"), P("series", "tm"))
    return jax.shard_map(local, mesh=mesh, in_specs=in_specs, out_specs=out_specs, check_vma=False)
```

```python
import jax
import jax.numpy as jnp
from jax import lax
from jax.experimental import pallas as pl
from jax.experimental.pallas import tpu as pltpu
from jax.sharding import PartitionSpec as P

MAXLAG = 168
ITERS = 2


def shifted(block, axis, distance):
    devices = range(lax.axis_size(axis))
    route = [(i - distance, i) for i in devices if i - distance in devices]
    return lax.ppermute(block, axis, route)


def exchange(block, axis, bit):
    devices = lax.axis_size(axis)
    return lax.ppermute(block, axis, [(i, i ^ bit) for i in range(devices)])


def butterfly_sum(block, axis):
    devices = lax.axis_size(axis)
    bit = 1
    while bit < devices:
        block = block + exchange(block, axis, bit)
        bit *= 2
    return block


def halving_sum(block, axis):
    devices = lax.axis_size(axis)
    position = lax.axis_index(axis)
    levels = devices.bit_length() - 1
    rows = block.shape[0] // devices
    block = block.reshape((2,) * levels + (rows,) + block.shape[1:])
    for level in range(levels):
        bit = 1 << level
        upper = (position & bit) != 0
        at = levels - 1 - level
        low = lax.index_in_dim(block, 0, at, keepdims=False)
        high = lax.index_in_dim(block, 1, at, keepdims=False)
        keep = jnp.where(upper, high, low)
        send = jnp.where(upper, low, high).astype(jnp.bfloat16)
        block = keep + exchange(send, axis, bit).astype(jnp.float32)
    return block


def doubling_gather(block, axis):
    devices = lax.axis_size(axis)
    position = lax.axis_index(axis)
    levels = devices.bit_length() - 1
    for step in range(levels):
        bit = 1 << (levels - 1 - step)
        upper = (position & bit) != 0
        other = exchange(block, axis, bit)
        low = jnp.where(upper, other, block)
        high = jnp.where(upper, block, other)
        block = jnp.stack([low, high], axis=step)
    return block.reshape((-1,) + block.shape[levels + 1 :])


def unpack(packed_words):
    shift_amounts = jnp.arange(8, dtype=jnp.int32)
    bit_values = jnp.right_shift(packed_words[:, :, None], shift_amounts) & 1
    return bit_values.reshape(packed_words.shape[0], packed_words.shape[1] * 8).astype(jnp.float32)


def lag_kernel(starts_ref, weights_ref, extended_ref, out_ref):
    width = out_ref.shape[0]
    running = jnp.zeros(out_ref.shape, jnp.float32)
    for k in range(weights_ref.shape[0]):
        row_block = extended_ref[pl.ds(starts_ref[k], width), :]
        running = running + weights_ref[pl.ds(k, 1), :] * row_block
    out_ref[...] = running


def lagged_sum(extended, weights, starts, width):
    rank = extended.shape[1]
    return pl.pallas_call(
        lag_kernel,
        out_shape=jax.ShapeDtypeStruct((width, rank), jnp.float32),
        in_specs=[
            pl.BlockSpec(memory_space=pltpu.SMEM),
            pl.BlockSpec(memory_space=pltpu.VMEM),
            pl.BlockSpec(memory_space=pltpu.VMEM),
        ],
        out_specs=pl.BlockSpec(memory_space=pltpu.VMEM),
        cost_estimate=pl.CostEstimate(
            flops=2 * weights.shape[0] * width * rank,
            transcendentals=0,
            bytes_accessed=4 * (extended.size + weights.size + width * rank),
        ),
    )(starts.astype(jnp.int32), weights, extended)


def fetch_rows(factors):
    return doubling_gather(factors.astype(jnp.bfloat16), "tm")


def local(panel, observed, series_factors, time_factors, ar_weights, lags):
    hours = panel.shape[1]
    total_hours = hours * lax.axis_size("tm")
    total_series = panel.shape[0] * lax.axis_size("series")
    mask_values = unpack(observed)
    position = lax.axis_index("tm")
    hour_index = position * hours + jnp.arange(hours, dtype=jnp.int32)
    active_rows = (hour_index >= MAXLAG)[:, None]

    def compute_misfit(rows_low, times_low):
        predicted = jnp.dot(rows_low, times_low, preferred_element_type=jnp.float32)
        return (mask_values * (predicted - panel.astype(jnp.float32))).astype(jnp.bfloat16)

    times = time_factors
    factors = series_factors
    for iteration in range(ITERS):
        rows_low = fetch_rows(factors)
        times_low = times.astype(jnp.bfloat16)
        misfit = compute_misfit(rows_low, times_low)
        grad_rows = halving_sum(
            lax.dot_general(
                misfit, times_low, (((1,), (1,)), ((), ())), preferred_element_type=jnp.float32
            ),
            "tm",
        )
        partial_value = lax.dot_general(
            rows_low, misfit, (((0,), (0,)), ((), ())), preferred_element_type=jnp.float32
        )
        grad_times = butterfly_sum(partial_value, "series")
        times_t = times.T
        tail_rows = shifted(times_t[hours - MAXLAG :], "tm", 1)
        errors = times_t - lagged_sum(
            jnp.concatenate([tail_rows, times_t], 0), ar_weights, MAXLAG - lags, hours
        )
        errors = jnp.where(active_rows, errors, 0.0)
        head_rows = shifted(errors[:MAXLAG], "tm", -1)
        ar_grad = (errors - lagged_sum(
            jnp.concatenate([errors, head_rows], 0), ar_weights, lags, hours
        )).T
        times_new = times - 24.0 / total_series * grad_times - 0.25 * ar_grad
        factors = factors - 2.0 / total_hours * grad_rows
        times = times_new
    final_rows = fetch_rows(factors)
    misfit_final = compute_misfit(final_rows, times.astype(jnp.bfloat16))
    return (factors, times, misfit_final)


def solution(mesh):
    in_specs = (
        P("series", "tm"),
        P("series", "tm"),
        P(("series", "tm"), None),
        P(None, "tm"),
        P(),
        P(),
    )
    out_specs = (P(("series", "tm"), None), P(None, "tm"), P("series", "tm"))
    return jax.shard_map(local, mesh=mesh, in_specs=in_specs, out_specs=out_specs, check_vma=False)
```

```python
import jax
import jax.numpy as jnp
from jax import lax
from jax.experimental import pallas as pl
from jax.experimental.pallas import tpu as pltpu
from jax.sharding import PartitionSpec as P

MAXLAG = 168
ITERS = 2


def shifted(block, axis, distance):
    devices = range(lax.axis_size(axis))
    route = [(i - distance, i) for i in devices if i - distance in devices]
    return lax.ppermute(block, axis, route)


def exchange(block, axis, bit):
    devices = lax.axis_size(axis)
    return lax.ppermute(block, axis, [(i, i ^ bit) for i in range(devices)])


def butterfly_sum(block, axis):
    devices = lax.axis_size(axis)
    bit = 1
    while bit < devices:
        block = block + exchange(block, axis, bit)
        bit *= 2
    return block


def halving_sum(block, axis):
    devices = lax.axis_size(axis)
    position = lax.axis_index(axis)
    levels = devices.bit_length() - 1
    rows = block.shape[0] // devices
    block = block.reshape((2,) * levels + (rows,) + block.shape[1:])
    for level in range(levels):
        bit = 1 << level
        upper = (position & bit) != 0
        at = levels - 1 - level
        low = lax.index_in_dim(block, 0, at, keepdims=False)
        high = lax.index_in_dim(block, 1, at, keepdims=False)
        keep = jnp.where(upper, high, low)
        send = jnp.where(upper, low, high).astype(jnp.bfloat16)
        block = keep + exchange(send, axis, bit).astype(jnp.float32)
    return block


def doubling_gather(block, axis):
    devices = lax.axis_size(axis)
    position = lax.axis_index(axis)
    levels = devices.bit_length() - 1
    for step in range(levels):
        bit = 1 << (levels - 1 - step)
        upper = (position & bit) != 0
        other = exchange(block, axis, bit)
        low = jnp.where(upper, other, block)
        high = jnp.where(upper, block, other)
        block = jnp.stack([low, high], axis=step)
    return block.reshape((-1,) + block.shape[levels + 1 :])


def unpack(packed_words):
    words = packed_words.shape[1]
    hour = jnp.arange(words * 8, dtype=jnp.int32)
    spread = (hour[None, :] // 8 == jnp.arange(words, dtype=jnp.int32)[:, None]).astype(jnp.bfloat16)
    repeated = jnp.dot(
        packed_words.astype(jnp.bfloat16), spread, preferred_element_type=jnp.float32
    ).astype(jnp.int32)
    return (jnp.right_shift(repeated, hour % 8) & 1).astype(jnp.float32)


def lag_kernel(starts_ref, weights_ref, extended_ref, out_ref):
    width = out_ref.shape[0]
    running = jnp.zeros(out_ref.shape, jnp.float32)
    for k in range(weights_ref.shape[0]):
        row_block = extended_ref[pl.ds(starts_ref[k], width), :]
        running = running + weights_ref[pl.ds(k, 1), :] * row_block
    out_ref[...] = running


def lagged_sum(extended, weights, starts, width):
    rank = extended.shape[1]
    return pl.pallas_call(
        lag_kernel,
        out_shape=jax.ShapeDtypeStruct((width, rank), jnp.float32),
        in_specs=[
            pl.BlockSpec(memory_space=pltpu.SMEM),
            pl.BlockSpec(memory_space=pltpu.VMEM),
            pl.BlockSpec(memory_space=pltpu.VMEM),
        ],
        out_specs=pl.BlockSpec(memory_space=pltpu.VMEM),
        cost_estimate=pl.CostEstimate(
            flops=2 * weights.shape[0] * width * rank,
            transcendentals=0,
            bytes_accessed=4 * (extended.size + weights.size + width * rank),
        ),
    )(starts.astype(jnp.int32), weights, extended)


def fetch_rows(factors):
    return doubling_gather(factors.astype(jnp.bfloat16), "tm")


def local(panel, observed, series_factors, time_factors, ar_weights, lags):
    hours = panel.shape[1]
    total_hours = hours * lax.axis_size("tm")
    total_series = panel.shape[0] * lax.axis_size("series")
    mask_values = unpack(observed)
    position = lax.axis_index("tm")
    hour_index = position * hours + jnp.arange(hours, dtype=jnp.int32)
    active_rows = (hour_index >= MAXLAG)[:, None]

    def compute_misfit(rows_low, times_low):
        predicted = jnp.dot(rows_low, times_low, preferred_element_type=jnp.float32)
        return (mask_values * (predicted - panel.astype(jnp.float32))).astype(jnp.bfloat16)

    times = time_factors
    factors = series_factors
    for iteration in range(ITERS):
        rows_low = fetch_rows(factors)
        times_low = times.astype(jnp.bfloat16)
        misfit = compute_misfit(rows_low, times_low)
        grad_rows = halving_sum(
            lax.dot_general(
                misfit, times_low, (((1,), (1,)), ((), ())), preferred_element_type=jnp.float32
            ),
            "tm",
        )
        partial_value = lax.dot_general(
            rows_low, misfit, (((0,), (0,)), ((), ())), preferred_element_type=jnp.float32
        )
        grad_times = butterfly_sum(partial_value, "series")
        times_t = times.T
        tail_rows = shifted(times_t[hours - MAXLAG :], "tm", 1)
        errors = times_t - lagged_sum(
            jnp.concatenate([tail_rows, times_t], 0), ar_weights, MAXLAG - lags, hours
        )
        errors = jnp.where(active_rows, errors, 0.0)
        head_rows = shifted(errors[:MAXLAG], "tm", -1)
        ar_grad = (errors - lagged_sum(
            jnp.concatenate([errors, head_rows], 0), ar_weights, lags, hours
        )).T
        times_new = times - 24.0 / total_series * grad_times - 0.25 * ar_grad
        factors = factors - 2.0 / total_hours * grad_rows
        times = times_new
    final_rows = fetch_rows(factors)
    misfit_final = compute_misfit(final_rows, times.astype(jnp.bfloat16))
    return (factors, times, misfit_final)


def solution(mesh):
    in_specs = (
        P("series", "tm"),
        P("series", "tm"),
        P(("series", "tm"), None),
        P(None, "tm"),
        P(),
        P(),
    )
    out_specs = (P(("series", "tm"), None), P(None, "tm"), P("series", "tm"))
    return jax.shard_map(local, mesh=mesh, in_specs=in_specs, out_specs=out_specs, check_vma=False)
```

```python
import jax
import jax.numpy as jnp
from jax import lax
from jax.experimental import pallas as pl
from jax.experimental.pallas import tpu as pltpu
from jax.sharding import PartitionSpec as P

MAXLAG = 168
ITERS = 2


def shifted(block, axis, distance):
    devices = range(lax.axis_size(axis))
    route = [(i - distance, i) for i in devices if i - distance in devices]
    return lax.ppermute(block, axis, route)


def exchange(block, axis, bit):
    devices = lax.axis_size(axis)
    return lax.ppermute(block, axis, [(i, i ^ bit) for i in range(devices)])


def butterfly_sum(block, axis):
    devices = lax.axis_size(axis)
    bit = 1
    while bit < devices:
        block = block + exchange(block, axis, bit)
        bit *= 2
    return block


def halving_sum(block, axis):
    devices = lax.axis_size(axis)
    position = lax.axis_index(axis)
    levels = devices.bit_length() - 1
    rows = block.shape[0] // devices
    block = block.reshape((2,) * levels + (rows,) + block.shape[1:])
    for level in range(levels):
        bit = 1 << level
        upper = (position & bit) != 0
        at = levels - 1 - level
        low = lax.index_in_dim(block, 0, at, keepdims=False)
        high = lax.index_in_dim(block, 1, at, keepdims=False)
        keep = jnp.where(upper, high, low)
        send = jnp.where(upper, low, high).astype(jnp.bfloat16)
        block = keep + exchange(send, axis, bit).astype(jnp.float32)
    return block


def doubling_gather(block, axis):
    devices = lax.axis_size(axis)
    position = lax.axis_index(axis)
    levels = devices.bit_length() - 1
    for step in range(levels):
        bit = 1 << (levels - 1 - step)
        upper = (position & bit) != 0
        other = exchange(block, axis, bit)
        low = jnp.where(upper, other, block)
        high = jnp.where(upper, block, other)
        block = jnp.stack([low, high], axis=step)
    return block.reshape((-1,) + block.shape[levels + 1 :])


def unpack(packed_words):
    words = packed_words.shape[1]
    hour = jnp.arange(words * 8, dtype=jnp.int32)
    spread = (hour[None, :] // 8 == jnp.arange(words, dtype=jnp.int32)[:, None]).astype(jnp.bfloat16)
    repeated = jnp.dot(
        packed_words.astype(jnp.bfloat16), spread, preferred_element_type=jnp.float32
    ).astype(jnp.int32)
    return (jnp.right_shift(repeated, hour % 8) & 1).astype(jnp.float32)


def lag_kernel(starts_ref, weights_ref, first_ref, second_ref, out_ref, window_ref):
    width, lead = out_ref.shape[0], first_ref.shape[0]
    window_ref[pl.ds(0, lead), :] = first_ref[...]
    window_ref[pl.ds(lead, second_ref.shape[0]), :] = second_ref[...]
    running = jnp.zeros(out_ref.shape, jnp.float32)
    for k in range(weights_ref.shape[0]):
        row_block = window_ref[pl.ds(starts_ref[k], width), :]
        running = running + weights_ref[pl.ds(k, 1), :] * row_block
    out_ref[...] = running


def lagged_sum(first, second, weights, starts, width):
    rows, rank = first.shape[0] + second.shape[0], first.shape[1]
    return pl.pallas_call(
        lag_kernel,
        out_shape=jax.ShapeDtypeStruct((width, rank), jnp.float32),
        in_specs=[
            pl.BlockSpec(memory_space=pltpu.SMEM),
            pl.BlockSpec(memory_space=pltpu.VMEM),
            pl.BlockSpec(memory_space=pltpu.VMEM),
            pl.BlockSpec(memory_space=pltpu.VMEM),
        ],
        out_specs=pl.BlockSpec(memory_space=pltpu.VMEM),
        scratch_shapes=[pltpu.VMEM((rows, rank), jnp.float32)],
        cost_estimate=pl.CostEstimate(
            flops=2 * weights.shape[0] * width * rank,
            transcendentals=0,
            bytes_accessed=4 * (rows * rank + weights.size + width * rank),
        ),
    )(starts.astype(jnp.int32), weights, first, second)


def fetch_rows(factors):
    return doubling_gather(factors.astype(jnp.bfloat16), "tm")


def local(panel, observed, series_factors, time_factors, ar_weights, lags):
    hours = panel.shape[1]
    total_hours = hours * lax.axis_size("tm")
    total_series = panel.shape[0] * lax.axis_size("series")
    mask_values = unpack(observed)
    position = lax.axis_index("tm")
    hour_index = position * hours + jnp.arange(hours, dtype=jnp.int32)
    active_rows = (hour_index >= MAXLAG)[:, None]

    def compute_misfit(rows_low, times_low):
        predicted = jnp.dot(rows_low, times_low, preferred_element_type=jnp.float32)
        return (mask_values * (predicted - panel.astype(jnp.float32))).astype(jnp.bfloat16)

    times = time_factors
    factors = series_factors
    for iteration in range(ITERS):
        rows_low = fetch_rows(factors)
        times_low = times.astype(jnp.bfloat16)
        misfit = compute_misfit(rows_low, times_low)
        grad_rows = halving_sum(
            lax.dot_general(
                misfit, times_low, (((1,), (1,)), ((), ())), preferred_element_type=jnp.float32
            ),
            "tm",
        )
        partial_value = lax.dot_general(
            rows_low, misfit, (((0,), (0,)), ((), ())), preferred_element_type=jnp.float32
        )
        grad_times = butterfly_sum(partial_value, "series")
        times_t = times.T
        tail_rows = shifted(times_t[hours - MAXLAG :], "tm", 1)
        errors = times_t - lagged_sum(tail_rows, times_t, ar_weights, MAXLAG - lags, hours)
        errors = jnp.where(active_rows, errors, 0.0)
        head_rows = shifted(errors[:MAXLAG], "tm", -1)
        ar_grad = (errors - lagged_sum(errors, head_rows, ar_weights, lags, hours)).T
        times_new = times - 24.0 / total_series * grad_times - 0.25 * ar_grad
        factors = factors - 2.0 / total_hours * grad_rows
        times = times_new
    final_rows = fetch_rows(factors)
    misfit_final = compute_misfit(final_rows, times.astype(jnp.bfloat16))
    return (factors, times, misfit_final)


def solution(mesh):
    in_specs = (
        P("series", "tm"),
        P("series", "tm"),
        P(("series", "tm"), None),
        P(None, "tm"),
        P(),
        P(),
    )
    out_specs = (P(("series", "tm"), None), P(None, "tm"), P("series", "tm"))
    return jax.shard_map(local, mesh=mesh, in_specs=in_specs, out_specs=out_specs, check_vma=False)
```

```python
import jax
import jax.numpy as jnp
from jax import lax
from jax.experimental import pallas as pl
from jax.experimental.pallas import tpu as pltpu
from jax.experimental.layout import Layout, with_layout_constraint
from jax.sharding import PartitionSpec as P

MAXLAG = 168
ITERS = 2


def shifted(block, axis, distance):
    devices = range(lax.axis_size(axis))
    route = [(i - distance, i) for i in devices if i - distance in devices]
    return lax.ppermute(block, axis, route)


def exchange(block, axis, bit):
    devices = lax.axis_size(axis)
    return lax.ppermute(block, axis, [(i, i ^ bit) for i in range(devices)])


def butterfly_sum(block, axis):
    devices = lax.axis_size(axis)
    bit = 1
    while bit < devices:
        block = block + exchange(block, axis, bit)
        bit *= 2
    return block


def halving_sum(block, axis):
    devices = lax.axis_size(axis)
    position = lax.axis_index(axis)
    levels = devices.bit_length() - 1
    rows = block.shape[0] // devices
    block = block.reshape((2,) * levels + (rows,) + block.shape[1:])
    for level in range(levels):
        bit = 1 << level
        upper = (position & bit) != 0
        at = levels - 1 - level
        low = lax.index_in_dim(block, 0, at, keepdims=False)
        high = lax.index_in_dim(block, 1, at, keepdims=False)
        keep = jnp.where(upper, high, low)
        send = jnp.where(upper, low, high).astype(jnp.bfloat16)
        block = keep + exchange(send, axis, bit).astype(jnp.float32)
    return block


def doubling_gather(block, axis):
    devices = lax.axis_size(axis)
    position = lax.axis_index(axis)
    levels = devices.bit_length() - 1
    for step in range(levels):
        bit = 1 << (levels - 1 - step)
        upper = (position & bit) != 0
        other = exchange(block, axis, bit)
        low = jnp.where(upper, other, block)
        high = jnp.where(upper, block, other)
        block = jnp.stack([low, high], axis=step)
    return block.reshape((-1,) + block.shape[levels + 1 :])


def unpack(packed_words):
    words = packed_words.shape[1]
    hour = jnp.arange(words * 8, dtype=jnp.int32)
    spread = (hour[None, :] // 8 == jnp.arange(words, dtype=jnp.int32)[:, None]).astype(jnp.bfloat16)
    repeated = jnp.dot(
        packed_words.astype(jnp.bfloat16), spread, preferred_element_type=jnp.float32
    ).astype(jnp.int32)
    return (jnp.right_shift(repeated, hour % 8) & 1).astype(jnp.float32)


def lag_total(window_ref, weights_ref, starts_ref, width):
    running = jnp.zeros((width, window_ref.shape[1]), jnp.float32)
    for k in range(weights_ref.shape[0]):
        row_block = window_ref[pl.ds(starts_ref[k], width), :]
        running = running + weights_ref[pl.ds(k, 1), :] * row_block
    return running


def error_kernel(scalars_ref, weights_ref, before_ref, times_ref, out_ref, window_ref):
    width = times_ref.shape[1]
    current = times_ref[...].T
    window_ref[pl.ds(0, width), :] = before_ref[...].T
    window_ref[pl.ds(width, width), :] = current
    errors = current - lag_total(window_ref, weights_ref, scalars_ref, width)
    hour = lax.broadcasted_iota(jnp.int32, errors.shape, 0) + scalars_ref[weights_ref.shape[0]]
    out_ref[...] = jnp.where(hour >= MAXLAG, errors, 0.0).T


def ar_kernel(scalars_ref, weights_ref, errors_ref, after_ref, out_ref, window_ref):
    width = errors_ref.shape[1]
    current = errors_ref[...].T
    window_ref[pl.ds(0, width), :] = current
    window_ref[pl.ds(width, width), :] = after_ref[...].T
    out_ref[...] = (current - lag_total(window_ref, weights_ref, scalars_ref, width)).T


def lag_call(kernel, scalars, weights, first, second):
    rank, width = first.shape
    return pl.pallas_call(
        kernel,
        out_shape=jax.ShapeDtypeStruct((rank, width), jnp.float32),
        in_specs=[
            pl.BlockSpec(memory_space=pltpu.SMEM),
            pl.BlockSpec(memory_space=pltpu.VMEM),
            pl.BlockSpec(memory_space=pltpu.VMEM),
            pl.BlockSpec(memory_space=pltpu.VMEM),
        ],
        out_specs=pl.BlockSpec(memory_space=pltpu.VMEM),
        scratch_shapes=[pltpu.VMEM((2 * width, rank), jnp.float32)],
        cost_estimate=pl.CostEstimate(
            flops=2 * weights.shape[0] * width * rank,
            transcendentals=0,
            bytes_accessed=4 * (3 * width * rank + weights.size),
        ),
    )(scalars, weights, first, second)


def fetch_rows(factors):
    return doubling_gather(factors.astype(jnp.bfloat16), "tm")


def local(panel, observed, series_factors, time_factors, ar_weights, lags):
    hours = panel.shape[1]
    total_hours = hours * lax.axis_size("tm")
    total_series = panel.shape[0] * lax.axis_size("series")
    mask_values = unpack(observed)
    position = lax.axis_index("tm")
    before_scalars = jnp.concatenate(
        [hours - lags.astype(jnp.int32), (position * hours)[None].astype(jnp.int32)]
    )
    after_scalars = lags.astype(jnp.int32)

    def compute_misfit(rows_low, times_low):
        predicted = jnp.dot(rows_low, times_low, preferred_element_type=jnp.float32)
        misfit = (mask_values * (predicted - panel.astype(jnp.float32))).astype(jnp.bfloat16)
        return with_layout_constraint(misfit, Layout((0, 1)))

    times = time_factors
    factors = series_factors
    for iteration in range(ITERS):
        rows_low = fetch_rows(factors)
        times_low = times.astype(jnp.bfloat16)
        misfit = compute_misfit(rows_low, times_low)
        grad_rows = halving_sum(
            lax.dot_general(
                misfit, times_low, (((1,), (1,)), ((), ())), preferred_element_type=jnp.float32
            ),
            "tm",
        )
        partial_value = lax.dot_general(
            rows_low, misfit, (((0,), (0,)), ((), ())), preferred_element_type=jnp.float32
        )
        grad_times = butterfly_sum(partial_value, "series")
        before_block = shifted(times, "tm", 1)
        errors = lag_call(error_kernel, before_scalars, ar_weights, before_block, times)
        after_block = shifted(errors, "tm", -1)
        ar_grad = lag_call(ar_kernel, after_scalars, ar_weights, errors, after_block)
        times_new = times - 24.0 / total_series * grad_times - 0.25 * ar_grad
        factors = factors - 2.0 / total_hours * grad_rows
        times = times_new
    final_rows = fetch_rows(factors)
    misfit_final = compute_misfit(final_rows, times.astype(jnp.bfloat16))
    return (factors, times, misfit_final)


def solution(mesh):
    in_specs = (
        P("series", "tm"),
        P("series", "tm"),
        P(("series", "tm"), None),
        P(None, "tm"),
        P(),
        P(),
    )
    out_specs = (P(("series", "tm"), None), P(None, "tm"), P("series", "tm"))
    return jax.shard_map(local, mesh=mesh, in_specs=in_specs, out_specs=out_specs, check_vma=False)
```

```python
import jax
import jax.numpy as jnp
from jax import lax
from jax.experimental import pallas as pl
from jax.experimental.pallas import tpu as pltpu
from jax.experimental.layout import Layout, with_layout_constraint
from jax.sharding import PartitionSpec as P

MAXLAG = 168
ITERS = 2


def shifted(block, axis, distance):
    devices = range(lax.axis_size(axis))
    route = [(i - distance, i) for i in devices if i - distance in devices]
    return lax.ppermute(block, axis, route)


def exchange(block, axis, bit):
    devices = lax.axis_size(axis)
    return lax.ppermute(block, axis, [(i, i ^ bit) for i in range(devices)])


def butterfly_sum(block, axis):
    devices = lax.axis_size(axis)
    bit = 1
    while bit < devices:
        block = block + exchange(block, axis, bit)
        bit *= 2
    return block


def halving_sum(block, axis):
    devices = lax.axis_size(axis)
    position = lax.axis_index(axis)
    levels = devices.bit_length() - 1
    rows = block.shape[0] // devices
    block = block.reshape((2,) * levels + (rows,) + block.shape[1:])
    for level in range(levels):
        bit = 1 << level
        upper = (position & bit) != 0
        at = levels - 1 - level
        low = lax.index_in_dim(block, 0, at, keepdims=False)
        high = lax.index_in_dim(block, 1, at, keepdims=False)
        keep = jnp.where(upper, high, low)
        send = jnp.where(upper, low, high).astype(jnp.bfloat16)
        block = keep + exchange(send, axis, bit).astype(jnp.float32)
    return block


def doubling_gather(block, axis, after=None):
    devices = lax.axis_size(axis)
    position = lax.axis_index(axis)
    levels = devices.bit_length() - 1
    for step in range(levels):
        if step == 1 and after is not None:
            block = block + (0.0 * after[:1, :1]).astype(block.dtype)
        bit = 1 << (levels - 1 - step)
        upper = (position & bit) != 0
        other = exchange(block, axis, bit)
        low = jnp.where(upper, other, block)
        high = jnp.where(upper, block, other)
        block = jnp.stack([low, high], axis=step)
    return block.reshape((-1,) + block.shape[levels + 1 :])


def unpack(packed_words):
    words = packed_words.shape[1]
    hour = jnp.arange(words * 8, dtype=jnp.int32)
    spread = (hour[None, :] // 8 == jnp.arange(words, dtype=jnp.int32)[:, None]).astype(jnp.bfloat16)
    repeated = jnp.dot(
        packed_words.astype(jnp.bfloat16), spread, preferred_element_type=jnp.float32
    ).astype(jnp.int32)
    return (jnp.right_shift(repeated, hour % 8) & 1).astype(jnp.float32)


def lag_total(window_ref, weights_ref, starts_ref, width):
    running = jnp.zeros((width, window_ref.shape[1]), jnp.float32)
    for k in range(weights_ref.shape[0]):
        row_block = window_ref[pl.ds(starts_ref[k], width), :]
        running = running + weights_ref[pl.ds(k, 1), :] * row_block
    return running


def error_kernel(scalars_ref, weights_ref, before_ref, times_ref, out_ref, window_ref):
    width = times_ref.shape[1]
    current = times_ref[...].T
    window_ref[pl.ds(0, width), :] = before_ref[...].T
    window_ref[pl.ds(width, width), :] = current
    errors = current - lag_total(window_ref, weights_ref, scalars_ref, width)
    hour = lax.broadcasted_iota(jnp.int32, errors.shape, 0) + scalars_ref[weights_ref.shape[0]]
    out_ref[...] = jnp.where(hour >= MAXLAG, errors, 0.0).T


def ar_kernel(scalars_ref, weights_ref, errors_ref, after_ref, out_ref, window_ref):
    width = errors_ref.shape[1]
    current = errors_ref[...].T
    window_ref[pl.ds(0, width), :] = current
    window_ref[pl.ds(width, width), :] = after_ref[...].T
    out_ref[...] = (current - lag_total(window_ref, weights_ref, scalars_ref, width)).T


def lag_call(kernel, scalars, weights, first, second):
    rank, width = first.shape
    return pl.pallas_call(
        kernel,
        out_shape=jax.ShapeDtypeStruct((rank, width), jnp.float32),
        in_specs=[
            pl.BlockSpec(memory_space=pltpu.SMEM),
            pl.BlockSpec(memory_space=pltpu.VMEM),
            pl.BlockSpec(memory_space=pltpu.VMEM),
            pl.BlockSpec(memory_space=pltpu.VMEM),
        ],
        out_specs=pl.BlockSpec(memory_space=pltpu.VMEM),
        scratch_shapes=[pltpu.VMEM((2 * width, rank), jnp.float32)],
        cost_estimate=pl.CostEstimate(
            flops=2 * weights.shape[0] * width * rank,
            transcendentals=0,
            bytes_accessed=4 * (3 * width * rank + weights.size),
        ),
    )(scalars, weights, first, second)


def fetch_rows(factors, after=None):
    return doubling_gather(factors.astype(jnp.bfloat16), "tm", after)


def local(panel, observed, series_factors, time_factors, ar_weights, lags):
    hours = panel.shape[1]
    total_hours = hours * lax.axis_size("tm")
    total_series = panel.shape[0] * lax.axis_size("series")
    mask_values = unpack(observed)
    position = lax.axis_index("tm")
    before_scalars = jnp.concatenate(
        [hours - lags.astype(jnp.int32), (position * hours)[None].astype(jnp.int32)]
    )
    after_scalars = lags.astype(jnp.int32)

    def compute_misfit(rows_low, times_low):
        predicted = jnp.dot(rows_low, times_low, preferred_element_type=jnp.float32)
        misfit = (mask_values * (predicted - panel.astype(jnp.float32))).astype(jnp.bfloat16)
        return with_layout_constraint(misfit, Layout((0, 1)))

    times = time_factors
    factors = series_factors
    for iteration in range(ITERS):
        rows_low = fetch_rows(factors)
        times_low = times.astype(jnp.bfloat16)
        misfit = compute_misfit(rows_low, times_low)
        grad_rows = halving_sum(
            lax.dot_general(
                misfit, times_low, (((1,), (1,)), ((), ())), preferred_element_type=jnp.float32
            ),
            "tm",
        )
        partial_value = lax.dot_general(
            rows_low, misfit, (((0,), (0,)), ((), ())), preferred_element_type=jnp.float32
        )
        grad_times = butterfly_sum(partial_value, "series")
        before_block = shifted(times, "tm", 1)
        errors = lag_call(error_kernel, before_scalars, ar_weights, before_block, times)
        after_block = shifted(errors, "tm", -1)
        ar_grad = lag_call(ar_kernel, after_scalars, ar_weights, errors, after_block)
        times_new = times - 24.0 / total_series * grad_times - 0.25 * ar_grad
        factors = factors - 2.0 / total_hours * grad_rows
        times = times_new
    final_rows = fetch_rows(factors, errors)
    misfit_final = compute_misfit(final_rows, times.astype(jnp.bfloat16))
    return (factors, times, misfit_final)


def solution(mesh):
    in_specs = (
        P("series", "tm"),
        P("series", "tm"),
        P(("series", "tm"), None),
        P(None, "tm"),
        P(),
        P(),
    )
    out_specs = (P(("series", "tm"), None), P(None, "tm"), P("series", "tm"))
    return jax.shard_map(local, mesh=mesh, in_specs=in_specs, out_specs=out_specs, check_vma=False)
```

```python
import jax
import jax.numpy as jnp
from jax import lax
from jax.experimental import pallas as pl
from jax.experimental.pallas import tpu as pltpu
from jax.experimental.layout import Layout, with_layout_constraint
from jax.sharding import PartitionSpec as P

MAXLAG = 168
ITERS = 2


def shifted(block, axis, distance):
    devices = range(lax.axis_size(axis))
    route = [(i - distance, i) for i in devices if i - distance in devices]
    return lax.ppermute(block, axis, route)


def exchange(block, axis, bit):
    devices = lax.axis_size(axis)
    return lax.ppermute(block, axis, [(i, i ^ bit) for i in range(devices)])


def butterfly_sum(block, axis):
    devices = lax.axis_size(axis)
    bit = 1
    while bit < devices:
        block = block + exchange(block, axis, bit)
        bit *= 2
    return block


def halving_sum(block, axis):
    devices = lax.axis_size(axis)
    position = lax.axis_index(axis)
    levels = devices.bit_length() - 1
    rows = block.shape[0] // devices
    block = block.reshape((2,) * levels + (rows,) + block.shape[1:])
    for level in range(levels):
        bit = 1 << level
        upper = (position & bit) != 0
        at = levels - 1 - level
        low = lax.index_in_dim(block, 0, at, keepdims=False)
        high = lax.index_in_dim(block, 1, at, keepdims=False)
        keep = jnp.where(upper, high, low)
        send = jnp.where(upper, low, high).astype(jnp.bfloat16)
        block = keep + exchange(send, axis, bit).astype(jnp.float32)
    return block


def doubling_gather(block, axis, after=None):
    devices = lax.axis_size(axis)
    position = lax.axis_index(axis)
    levels = devices.bit_length() - 1
    for step in range(levels):
        if step == 1 and after is not None:
            block = block + (0.0 * after[:1, :1]).astype(block.dtype)
        bit = 1 << (levels - 1 - step)
        upper = (position & bit) != 0
        other = exchange(block, axis, bit)
        low = jnp.where(upper, other, block)
        high = jnp.where(upper, block, other)
        block = jnp.stack([low, high], axis=step)
    return block.reshape((-1,) + block.shape[levels + 1 :])


def unpack(packed_words):
    words = packed_words.shape[1]
    hour = jnp.arange(words * 8, dtype=jnp.int32)
    spread = (hour[None, :] // 8 == jnp.arange(words, dtype=jnp.int32)[:, None]).astype(jnp.bfloat16)
    repeated = jnp.dot(
        packed_words.astype(jnp.bfloat16), spread, preferred_element_type=jnp.float32
    ).astype(jnp.int32)
    return (jnp.right_shift(repeated, hour % 8) & 1).astype(jnp.float32)


def lag_total(window_ref, weights_ref, starts_ref, width):
    running = jnp.zeros((width, window_ref.shape[1]), jnp.float32)
    for k in range(weights_ref.shape[0]):
        row_block = window_ref[pl.ds(starts_ref[k], width), :]
        running = running + weights_ref[pl.ds(k, 1), :] * row_block
    return running


def error_kernel(scalars_ref, weights_ref, before_ref, times_ref, out_ref, window_ref):
    width = times_ref.shape[1]
    current = times_ref[...].T
    window_ref[pl.ds(0, width), :] = before_ref[...].T
    window_ref[pl.ds(width, width), :] = current
    errors = current - lag_total(window_ref, weights_ref, scalars_ref, width)
    hour = lax.broadcasted_iota(jnp.int32, errors.shape, 0) + scalars_ref[weights_ref.shape[0]]
    out_ref[...] = jnp.where(hour >= MAXLAG, errors, 0.0).T


def ar_kernel(scalars_ref, weights_ref, errors_ref, after_ref, out_ref, window_ref):
    width = errors_ref.shape[1]
    current = errors_ref[...].T
    window_ref[pl.ds(0, width), :] = current
    window_ref[pl.ds(width, width), :] = after_ref[...].T
    out_ref[...] = (current - lag_total(window_ref, weights_ref, scalars_ref, width)).T


def lag_call(kernel, scalars, weights, first, second):
    rank, width = first.shape
    return pl.pallas_call(
        kernel,
        out_shape=jax.ShapeDtypeStruct((rank, width), jnp.float32),
        in_specs=[
            pl.BlockSpec(memory_space=pltpu.SMEM),
            pl.BlockSpec(memory_space=pltpu.VMEM),
            pl.BlockSpec(memory_space=pltpu.VMEM),
            pl.BlockSpec(memory_space=pltpu.VMEM),
        ],
        out_specs=pl.BlockSpec(memory_space=pltpu.VMEM),
        scratch_shapes=[pltpu.VMEM((2 * width, rank), jnp.float32)],
        cost_estimate=pl.CostEstimate(
            flops=2 * weights.shape[0] * width * rank,
            transcendentals=0,
            bytes_accessed=4 * (3 * width * rank + weights.size),
        ),
    )(scalars, weights, first, second)


def fetch_rows(factors, after=None):
    return doubling_gather(factors.astype(jnp.bfloat16), "tm", after)


def local(panel, observed, series_factors, time_factors, ar_weights, lags):
    hours = panel.shape[1]
    total_hours = hours * lax.axis_size("tm")
    total_series = panel.shape[0] * lax.axis_size("series")
    mask_values = unpack(observed)
    position = lax.axis_index("tm")
    before_scalars = jnp.concatenate(
        [hours - lags.astype(jnp.int32), (position * hours)[None].astype(jnp.int32)]
    )
    after_scalars = lags.astype(jnp.int32)

    def compute_misfit(rows_low, times_low):
        predicted = jnp.dot(rows_low, times_low, preferred_element_type=jnp.float32)
        misfit = (mask_values * (predicted - panel.astype(jnp.float32))).astype(jnp.bfloat16)
        return with_layout_constraint(misfit, Layout((0, 1)))

    times = time_factors
    factors = series_factors
    for iteration in range(ITERS):
        before_block = shifted(times, "tm", 1)
        errors = lag_call(error_kernel, before_scalars, ar_weights, before_block, times)
        rows_low = fetch_rows(factors, errors if iteration == 0 else None)
        times_low = times.astype(jnp.bfloat16)
        misfit = compute_misfit(rows_low, times_low)
        grad_rows = halving_sum(
            lax.dot_general(
                misfit, times_low, (((1,), (1,)), ((), ())), preferred_element_type=jnp.float32
            ),
            "tm",
        )
        partial_value = lax.dot_general(
            rows_low, misfit, (((0,), (0,)), ((), ())), preferred_element_type=jnp.float32
        )
        grad_times = butterfly_sum(partial_value, "series")
        after_block = shifted(errors, "tm", -1)
        ar_grad = lag_call(ar_kernel, after_scalars, ar_weights, errors, after_block)
        times_new = times - 24.0 / total_series * grad_times - 0.25 * ar_grad
        factors = factors - 2.0 / total_hours * grad_rows
        times = times_new
    final_rows = fetch_rows(factors, errors)
    misfit_final = compute_misfit(final_rows, times.astype(jnp.bfloat16))
    return (factors, times, misfit_final)


def solution(mesh):
    in_specs = (
        P("series", "tm"),
        P("series", "tm"),
        P(("series", "tm"), None),
        P(None, "tm"),
        P(),
        P(),
    )
    out_specs = (P(("series", "tm"), None), P(None, "tm"), P("series", "tm"))
    return jax.shard_map(local, mesh=mesh, in_specs=in_specs, out_specs=out_specs, check_vma=False)
```
